512 devices in a mesh: chan: 128 (over z, y, core), win: 4 (over x).
Axes of the slice: x: 4, y: 8, z: 8, core: 2. Of those that a mesh axis runs over, the one named last changes fastest.
Arguments:
- traces: bfloat16 [4, 8192, 2048], P('win', 'chan'), may hold values from -6 to 6
- round_masks: int32 [2], replicated, may hold values from 1 to 127, as said below
- row_owner: int32 [49152, 1], P('chan'), may hold values from 0 to 127; in each aligned block of 384 rows (0 to 383, 384 to 767, ...) at most 6 rows name the same one
- row_slot: int32 [49152], P('chan'), may hold values from 0 to 3
Outputs:
- binned: float32 [512, 1024], P('chan', 'win')
The draws below stay inside these ranges and needn't reach their ends.
Inputs may be any that keep to these rules, and one draw needn't show every extreme that they name: `round_masks`: all different; group g is matched in round r with group g XOR round_masks[r]. One of the rounds has the mask 128 - 1. `row_owner`: among the 384 pairs of one channel group no owner is named more than 6 times, a bound that some block reaches.
All inputs are finite; a program needn't handle non-finite values.
Results may differ from the reference program's by a relative error of at most 0.0039.
Values may be sent and summed in bfloat16 or wider, within the bound.
No kernel may reach another device: no remote copies, remote signals or barrier semaphores. Data moves between devices by JAX's collectives and lax.ppermute only.
A program may use at most 64 MiB of HBM per device.

```python
import math
import jax
import jax.numpy as jnp
import numpy as np
from jax import lax

CH = 64
S = 2048
LAG = 512
SRC = 2
ROUNDS = 2
BINCAP = 4
CHANNELS = 8192
WINDOWS = 4
SETS = 3
ROWS_DEV = 384
NBINS = 512
CAPR = 6
N_CHAN = 128


def draw_round_masks(key, part):
    first_key = jax.random.fold_in(key, 11)
    second_key = jax.random.fold_in(key, 23)
    others = (jax.random.permutation(first_key, N_CHAN - 2) + 1).astype(jnp.int32)
    values = jnp.concatenate([jnp.full((1,), N_CHAN - 1, jnp.int32), others[:ROUNDS - 1]])
    order = jax.random.permutation(second_key, ROUNDS)
    return values[order].astype(jnp.int32)


def set_ends(entries, stream_key, least, largest):
    dims = entries.shape
    index_at = [jax.random.randint(jax.random.fold_in(stream_key, axis), (), 0, dims[axis]) for axis in range(len(dims))]
    entries = entries.at[tuple(index_at)].set(least)
    longest = dims.index(max(dims))
    index_at[longest] = (index_at[longest] + 1) % dims[longest]
    return entries.at[tuple(index_at)].set(largest)


def block_scale(own_key, shape, pieces, smallest, high):
    gain, own = 1.0, jax.random.fold_in(own_key, 6)
    for axis_at, blocks in pieces:
        draws = jnp.exp(jax.random.uniform(jax.random.fold_in(own, axis_at), (blocks,), jnp.float32, smallest / len(pieces), high / len(pieces)))
        gain = gain * jnp.repeat(draws, shape[axis_at] // blocks).reshape([-1 if axis == axis_at else 1 for axis in range(len(shape))])
    return gain


def routed_block(stream_key, own, number, rows, count, top, limit, skew):
    sequence = jax.random.permutation(stream_key, count)
    crowded, common = portions_of(count, rows * top, limit, skew, True), portions_of(count, rows * top, limit, skew, False)
    places = jnp.arange(count)

    def named(sizes, turn):
        used = int((sizes > 0).sum())
        fixed = max(1, used // 4)
        shifted = fixed + (places - fixed + turn * (used - fixed)) % max(1, count - fixed)
        return jnp.zeros((count,), jnp.int32).at[sequence[jnp.where(places < fixed, places, shifted)]].set(jnp.asarray(sizes, jnp.int32))

    sizes = jnp.where(number % 4 == 0, named(crowded, number // 4), named(common, number - number // 4 - 1))
    mixed = jax.random.permutation(jax.random.fold_in(own, 3), count)
    giver, taker = mixed[0:count // 2 * 2:2], mixed[1:count // 2 * 2:2]
    slack = jnp.minimum(sizes[giver] - 1, limit - sizes[taker]) // 2
    slack = jnp.where((giver == sequence[0]) | (taker == sequence[0]) | (sizes[taker] == 0), 0, jnp.maximum(slack, 0))
    shifted = jax.random.randint(jax.random.fold_in(own, 4), (count // 2,), 0, 1 << 20) % (slack + 1)
    sizes = sizes.at[giver].add(-shifted).at[taker].add(shifted)
    items = jnp.searchsorted(jnp.cumsum(sizes), jnp.arange(rows * top), side="right").astype(jnp.int32)
    listing = items.reshape(top, rows).T
    listing = listing[jax.random.permutation(jax.random.fold_in(own, 1), rows)]
    turn = jax.random.randint(jax.random.fold_in(own, 2), (rows, 1), 0, top)
    return jnp.take_along_axis(listing, (jnp.arange(top)[None, :] + turn) % top, axis=1)


def portions_of(count, total, bound, skew, full):
    portions = [(1 << 20) // math.isqrt(rank ** skew) + 1 for rank in range(1, count + 1)]
    largest = bound if full else min(bound, max(-(-total // count), total * portions[0] // sum(portions)))
    least = 1 if total - largest >= count - 1 else 0
    given, spare = [largest] + [least] * (count - 1), total - largest - least * (count - 1)
    while spare > 0:
        free = [i for i in range(1, count) if given[i] < largest] or [i for i in range(1, count) if given[i] < bound]
        whole, remaining = sum([portions[i] for i in free]), spare
        for i in free:
            more = min(bound - given[i], max(1, remaining * portions[i] // whole), spare)
            given[i] = given[i] + more
            spare = spare - more
    return np.array(given)


def normal_values(stream_key, extent, scale, bound, cuts=(), kind=jnp.bfloat16):
    entries = scale * jax.random.normal(stream_key, extent, jnp.float32)
    if cuts:
        entries = entries * block_scale(stream_key, extent, cuts, -0.22, 0.18)
    return jnp.clip(entries, -bound, bound).astype(kind)


def setup_inputs(seed: int = 0) -> dict:
    key_of = jax.random.split(jax.random.key(seed), 5)
    traces = normal_values(key_of[0], (WINDOWS, CHANNELS, S), 1.0, 6.0, ((0, 4), (1, 128)))
    round_masks = draw_round_masks(jax.random.fold_in(key_of[4], 71), 0)
    row_owner_keys = jax.random.split(jax.random.fold_in(key_of[2], 1), (N_CHAN * ROWS_DEV) // ROWS_DEV)
    row_owner_turns = jax.random.permutation(jax.random.fold_in(key_of[2], 3), (N_CHAN * ROWS_DEV) // ROWS_DEV)
    row_owner = jax.vmap(lambda own, number: routed_block(jax.random.fold_in(key_of[2], 2), own, number, ROWS_DEV, N_CHAN, 1, CAPR, 2))(row_owner_keys, row_owner_turns).reshape((N_CHAN * ROWS_DEV, 1))
    row_slot = set_ends(jax.random.randint(key_of[3], (N_CHAN * ROWS_DEV,), 0, BINCAP), jax.random.fold_in(key_of[3], 1), 0, BINCAP - 1).astype(jnp.int32)
    return dict(traces=traces, round_masks=round_masks, row_owner=row_owner, row_slot=row_slot)


def normalize(traces):
    data = traces.astype(jnp.float32)
    scale = lax.rsqrt(lax.optimization_barrier(jnp.mean(data * data, axis=-1, keepdims=True)) + 1e-06)
    return (data * scale).astype(jnp.bfloat16)

def reference(traces, round_masks, row_owner, row_slot):
    normed = normalize(traces).astype(jnp.float32)
    length = 2 * S
    stride = CH // SRC
    bins = (row_owner[:, 0] * BINCAP + row_slot).astype(jnp.int32)

    def group_rows(group):
        own = lax.dynamic_slice_in_dim(normed, group * CH, CH, 1)
        sources = own[:, ::stride, :]
        partners = jnp.concatenate([group[None], jnp.bitwise_xor(group, round_masks)]).astype(jnp.int32)
        receivers = jnp.stack([lax.dynamic_slice_in_dim(normed, partners[i] * CH, CH, 1) for i in range(SETS)])
        source_spec = jnp.fft.rfft(sources, n=length, axis=-1)
        receiver_spec = jnp.fft.rfft(receivers, n=length, axis=-1)
        cross = lax.optimization_barrier(jnp.sum(jnp.conj(source_spec)[None, :, :, None, :] * receiver_spec[:, :, None, :, :], axis=1))
        lagged = jnp.fft.irfft(cross, n=length, axis=-1)
        window = jnp.concatenate([lagged[..., length - LAG:], lagged[..., :LAG]], axis=-1)
        return window.reshape(ROWS_DEV, 2 * LAG) / jnp.sqrt(jnp.float32(S))

    def accumulate(total, group):
        rows = group_rows(group)
        labels = lax.dynamic_slice_in_dim(bins, group * ROWS_DEV, ROWS_DEV, 0)
        return (total + jax.ops.segment_sum(rows, labels, num_segments=NBINS), None)
    groups = jnp.arange(N_CHAN, dtype=jnp.int32)
    sums, _ = lax.scan(accumulate, jnp.zeros((NBINS, 2 * LAG), jnp.float32), groups)
    counts = jax.ops.segment_sum(jnp.ones(bins.shape, jnp.float32), bins, num_segments=NBINS)
    return sums / jnp.sqrt(jnp.maximum(counts, 1.0))[:, None]
```

```python
import jax
import jax.numpy as jnp
from jax import lax
from jax.sharding import PartitionSpec as P

LAG = 512
SRC = 2
ROUNDS = 2
BINCAP = 4


block_width = 128


def normalize(traces):
    data = traces.astype(jnp.float32)
    scale = lax.rsqrt(jnp.mean(data * data, axis=-1, keepdims=True) + 1e-06)
    return (data * scale).astype(jnp.bfloat16)


def source_toeplitz(source):
    blocks = source.reshape(-1, block_width)
    padded = jnp.concatenate(
        [blocks, jnp.zeros((blocks.shape[0], block_width + 1), blocks.dtype)], axis=1
    )
    tiled = jnp.tile(padded, (1, block_width))
    return tiled[:, : 2 * block_width * block_width].reshape(
        blocks.shape[0], block_width, 2 * block_width
    )


def correlate(receivers, toeplitz):
    chans, samples = receivers.shape
    quota = samples // block_width
    lag_blocks = 2 * LAG // block_width
    extended = jnp.pad(receivers, ((0, 0), (LAG, LAG + block_width)))
    cells = extended.reshape(chans, -1, block_width)
    doubled = jnp.concatenate([cells[:, :-1], cells[:, 1:]], axis=-1)
    parts = [
        jnp.einsum(
            "cqw,sqrw->scr",
            doubled[:, p : p + quota],
            toeplitz,
            preferred_element_type=jnp.float32,
        )
        for p in range(lag_blocks)
    ]
    return jnp.concatenate(parts, axis=-1)


def bit_groups(bits):
    groups = [(0, 1)] if bits > 0 else []
    start = 1
    while start < bits:
        width = min(3, bits - start)
        groups.append((start, width))
        start += width
    return groups[1:] + groups[:1]


def exchange(payload, masks, axis):
    n = lax.axis_size(axis)
    bits = n.bit_length() - 1
    for shift, width in bit_groups(bits):
        options = [payload]
        for d in range(1, 1 << width):
            step = d << shift
            options.append(lax.ppermute(payload, axis, [(i, i ^ step) for i in range(n)]))
        stacked = jnp.stack(options)
        picks = jnp.bitwise_and(jnp.right_shift(masks, shift), (1 << width) - 1)
        payload = jnp.stack([stacked[picks[r], r] for r in range(masks.shape[0])])
    return payload


def body(traces, round_masks, row_owner, row_slot):
    wins, chans, samples = traces.shape
    rows_set = SRC * chans
    normed = normalize(traces)[0]
    stride = chans // SRC
    sources = normed[::stride, :]
    owner = row_owner[:, 0]
    slot = row_slot
    label_rows = []
    for r in range(ROUNDS):
        part = slice((r + 1) * rows_set, (r + 2) * rows_set)
        row = jnp.concatenate([owner[part], slot[part]]).astype(jnp.bfloat16)
        row = jnp.pad(row, (0, samples - row.shape[0]))
        label_rows.append(jnp.concatenate([sources, row[None, :]], axis=0))
    payload = jnp.stack(label_rows)
    arrived = exchange(payload, round_masks, "chan")
    all_sources = jnp.concatenate([sources] + [arrived[r, :SRC] for r in range(ROUNDS)], axis=0)
    toeplitz = jax.vmap(source_toeplitz)(all_sources)
    rows = correlate(normed, toeplitz).reshape(-1, 2 * LAG) / jnp.sqrt(jnp.float32(samples))
    rows = lax.psum_scatter(rows, "win", scatter_dimension=1, tiled=True)
    owners_total = lax.axis_size("chan")
    nbins = owners_total * BINCAP
    bins_parts = [owner[:rows_set] * BINCAP + slot[:rows_set]]
    for r in range(ROUNDS):
        got = arrived[r, SRC].astype(jnp.int32)
        bins_parts.append(got[:rows_set] * BINCAP + got[rows_set : 2 * rows_set])
    bins = jnp.concatenate(bins_parts)
    picks = (bins[None, :] == jnp.arange(nbins, dtype=jnp.int32)[:, None]).astype(jnp.float32)
    local = jnp.dot(picks, rows, precision=lax.Precision.HIGHEST, preferred_element_type=jnp.float32)
    sums = lax.psum_scatter(local, "chan", scatter_dimension=0, tiled=True)
    own_bins = owner * BINCAP + slot
    own_counts = jnp.sum(
        (own_bins[None, :] == jnp.arange(nbins, dtype=jnp.int32)[:, None]).astype(jnp.float32), axis=1
    )
    counts = lax.psum_scatter(own_counts, "chan", scatter_dimension=0, tiled=True)
    return sums / jnp.sqrt(jnp.maximum(counts, 1.0))[:, None]


def solution(mesh):
    return jax.shard_map(
        body,
        mesh=mesh,
        in_specs=(P("win", "chan", None), P(), P("chan", None), P("chan")),
        out_specs=P("chan", "win"),
        check_vma=False,
    )
```

```python
import jax
import jax.numpy as jnp
from jax import lax
from jax.sharding import PartitionSpec as P

LAG = 512
SRC = 2
ROUNDS = 2
BINCAP = 4


block_width = 128


def normalize(traces):
    data = traces.astype(jnp.float32)
    scale = lax.rsqrt(jnp.mean(data * data, axis=-1, keepdims=True) + 1e-06)
    return (data * scale).astype(jnp.bfloat16)


def source_toeplitz(source):
    blocks = source.reshape(-1, block_width)
    padded = jnp.concatenate(
        [blocks, jnp.zeros((blocks.shape[0], block_width + 1), blocks.dtype)], axis=1
    )
    tiled = jnp.tile(padded, (1, block_width))
    return tiled[:, : 2 * block_width * block_width].reshape(
        blocks.shape[0], block_width, 2 * block_width
    )


def correlate(receivers, toeplitz):
    chans, samples = receivers.shape
    quota = samples // block_width
    lag_blocks = 2 * LAG // block_width
    extended = jnp.pad(receivers, ((0, 0), (LAG, LAG + block_width)))
    cells = extended.reshape(chans, -1, block_width)
    doubled = jnp.concatenate([cells[:, :-1], cells[:, 1:]], axis=-1)
    parts = [
        jnp.einsum(
            "cqw,sqrw->scr",
            doubled[:, p : p + quota],
            toeplitz,
            preferred_element_type=jnp.float32,
        )
        for p in range(lag_blocks)
    ]
    return jnp.concatenate(parts, axis=-1)


def xor_permute(x, mask, axis, shift, width):
    n = lax.axis_size(axis)

    def moved(step):
        return lambda v: lax.ppermute(v, axis, [(i, i ^ step) for i in range(n)])

    branches = [lambda v: v] + [moved(d << shift) for d in range(1, 1 << width)]
    part = jnp.bitwise_and(jnp.right_shift(mask, shift), (1 << width) - 1)
    return lax.switch(part, branches, x)


def exchange(payload, masks, axis):
    n = lax.axis_size(axis)
    bits = n.bit_length() - 1
    full = n - 1
    first_full = masks[0] == full
    other = jnp.bitwise_xor(jnp.bitwise_xor(masks[0], masks[1]), full)
    fixed = jnp.where(first_full, payload[0], payload[1])
    free = jnp.where(first_full, payload[1], payload[0])
    fixed = lax.ppermute(fixed, axis, [(i, i ^ full) for i in range(n)])
    low = min(bits, 4)
    free = xor_permute(free, other, axis, 0, low)
    if bits > low:
        free = xor_permute(free, other, axis, low, bits - low)
    return jnp.stack(
        [jnp.where(first_full, fixed, free), jnp.where(first_full, free, fixed)]
    )


def body(traces, round_masks, row_owner, row_slot):
    wins, chans, samples = traces.shape
    rows_set = SRC * chans
    normed = normalize(traces)[0]
    stride = chans // SRC
    sources = normed[::stride, :]
    owner = row_owner[:, 0]
    slot = row_slot
    label_rows = []
    for r in range(ROUNDS):
        part = slice((r + 1) * rows_set, (r + 2) * rows_set)
        row = jnp.concatenate([owner[part], slot[part]]).astype(jnp.bfloat16)
        row = jnp.pad(row, (0, samples - row.shape[0]))
        label_rows.append(jnp.concatenate([sources, row[None, :]], axis=0))
    payload = jnp.stack(label_rows)
    arrived = exchange(payload, round_masks, "chan")
    all_sources = jnp.concatenate([sources] + [arrived[r, :SRC] for r in range(ROUNDS)], axis=0)
    toeplitz = jax.vmap(source_toeplitz)(all_sources)
    rows = correlate(normed, toeplitz).reshape(-1, 2 * LAG) / jnp.sqrt(jnp.float32(samples))
    rows = lax.psum_scatter(rows, "win", scatter_dimension=1, tiled=True)
    owners_total = lax.axis_size("chan")
    nbins = owners_total * BINCAP
    bins_parts = [owner[:rows_set] * BINCAP + slot[:rows_set]]
    for r in range(ROUNDS):
        got = arrived[r, SRC].astype(jnp.int32)
        bins_parts.append(got[:rows_set] * BINCAP + got[rows_set : 2 * rows_set])
    bins = jnp.concatenate(bins_parts)
    picks = (bins[None, :] == jnp.arange(nbins, dtype=jnp.int32)[:, None]).astype(jnp.float32)
    local = jnp.dot(picks, rows, precision=lax.Precision.HIGHEST, preferred_element_type=jnp.float32)
    arrived_sums = lax.all_to_all(local, "chan", split_axis=0, concat_axis=0, tiled=True)
    sums = jnp.sum(arrived_sums.reshape(owners_total, BINCAP, -1), axis=0)
    own_bins = owner * BINCAP + slot
    own_counts = jnp.sum(
        (own_bins[None, :] == jnp.arange(nbins, dtype=jnp.int32)[:, None]).astype(jnp.float32), axis=1
    )
    arrived_counts = lax.all_to_all(own_counts, "chan", split_axis=0, concat_axis=0, tiled=True)
    counts = jnp.sum(arrived_counts.reshape(owners_total, BINCAP), axis=0)
    return sums / jnp.sqrt(jnp.maximum(counts, 1.0))[:, None]


def solution(mesh):
    return jax.shard_map(
        body,
        mesh=mesh,
        in_specs=(P("win", "chan", None), P(), P("chan", None), P("chan")),
        out_specs=P("chan", "win"),
        check_vma=False,
    )
```

```python
import jax
import jax.numpy as jnp
from jax import lax
from jax.sharding import PartitionSpec as P
from jax.experimental import pallas as pl
from jax.experimental.pallas import tpu as pltpu

LAG = 512
SRC = 2
ROUNDS = 2
BINCAP = 4


block_width = 128


def normalize(traces):
    data = traces.astype(jnp.float32)
    scale = lax.rsqrt(jnp.mean(data * data, axis=-1, keepdims=True) + 1e-06)
    return (data * scale).astype(jnp.bfloat16)


def toeplitz_kernel(src_ref, out_ref):
    for q in range(out_ref.shape[1]):
        row = src_ref[0, q : q + 1, :].astype(jnp.float32)
        row = jnp.concatenate([row, jnp.zeros_like(row)], axis=1)
        band = jnp.broadcast_to(row, (block_width, 2 * block_width))
        out_ref[0, q] = pltpu.roll(band, 0, 1, stride=1, stride_axis=0).astype(out_ref.dtype)


def source_toeplitz(sources):
    n, samples = sources.shape
    quota = samples // block_width
    blocks = sources.reshape(n, quota, block_width)
    return pl.pallas_call(
        toeplitz_kernel,
        grid=(n,),
        in_specs=[pl.BlockSpec((1, quota, block_width), lambda s: (s, 0, 0))],
        out_specs=pl.BlockSpec((1, quota, block_width, 2 * block_width), lambda s: (s, 0, 0, 0)),
        out_shape=jax.ShapeDtypeStruct((n, quota, block_width, 2 * block_width), sources.dtype),
    )(blocks)


def receiver_windows(receivers):
    chans, samples = receivers.shape
    quota = samples // block_width
    lag_blocks = 2 * LAG // block_width
    extended = jnp.pad(receivers, ((0, 0), (LAG, LAG + block_width)))
    cells = extended.reshape(chans, -1, block_width)
    doubled = jnp.concatenate([cells[:, :-1], cells[:, 1:]], axis=-1)
    return jnp.stack([doubled[:, p : p + quota] for p in range(lag_blocks)], axis=1)


def correlate(windows, toeplitz):
    return jnp.einsum("cpqw,sqrw->scpr", windows, toeplitz, preferred_element_type=jnp.float32)


def xor_permute(x, mask, axis, shift, width):
    n = lax.axis_size(axis)

    def moved(step):
        return lambda v: lax.ppermute(v, axis, [(i, i ^ step) for i in range(n)])

    branches = [lambda v: v] + [moved(d << shift) for d in range(1, 1 << width)]
    part = jnp.bitwise_and(jnp.right_shift(mask, shift), (1 << width) - 1)
    return lax.switch(part, branches, x)


def exchange(payload, masks, axis):
    n = lax.axis_size(axis)
    bits = n.bit_length() - 1
    full = n - 1
    first_full = masks[0] == full
    other = jnp.bitwise_xor(jnp.bitwise_xor(masks[0], masks[1]), full)
    fixed = jnp.where(first_full, payload[0], payload[1])
    free = jnp.where(first_full, payload[1], payload[0])
    fixed = lax.ppermute(fixed, axis, [(i, i ^ full) for i in range(n)])
    low = min(bits, 4)
    free = xor_permute(free, other, axis, 0, low)
    if bits > low:
        free = xor_permute(free, other, axis, low, bits - low)
    return jnp.stack(
        [jnp.where(first_full, fixed, free), jnp.where(first_full, free, fixed)]
    )


def body(traces, round_masks, row_owner, row_slot):
    wins, chans, samples = traces.shape
    rows_set = SRC * chans
    normed = normalize(traces)[0]
    stride = chans // SRC
    sources = normed[::stride, :]
    owner = row_owner[:, 0]
    slot = row_slot
    label_rows = []
    for r in range(ROUNDS):
        part = slice((r + 1) * rows_set, (r + 2) * rows_set)
        row = jnp.concatenate([owner[part], slot[part]]).astype(jnp.bfloat16)
        row = jnp.pad(row, (0, samples - row.shape[0]))
        label_rows.append(jnp.concatenate([sources, row[None, :]], axis=0))
    payload = jnp.stack(label_rows)
    arrived = exchange(payload, round_masks, "chan")
    windows = receiver_windows(normed)
    scale = 1.0 / jnp.sqrt(jnp.float32(samples))
    own = correlate(windows, source_toeplitz(sources))
    partners = jnp.concatenate([arrived[r, :SRC] for r in range(ROUNDS)], axis=0)
    far = correlate(windows, source_toeplitz(partners))
    rows = jnp.concatenate([own, far], axis=0) * scale
    rows = rows.reshape(-1, 2 * LAG)
    rows = lax.psum_scatter(rows, "win", scatter_dimension=1, tiled=True)
    owners_total = lax.axis_size("chan")
    nbins = owners_total * BINCAP
    bins_parts = [owner[:rows_set] * BINCAP + slot[:rows_set]]
    for r in range(ROUNDS):
        got = arrived[r, SRC].astype(jnp.int32)
        bins_parts.append(got[:rows_set] * BINCAP + got[rows_set : 2 * rows_set])
    bins = jnp.concatenate(bins_parts)
    picks = (bins[None, :] == jnp.arange(nbins, dtype=jnp.int32)[:, None]).astype(jnp.float32)
    local = jnp.dot(picks, rows, precision=lax.Precision.HIGHEST, preferred_element_type=jnp.float32)
    arrived_sums = lax.all_to_all(local, "chan", split_axis=0, concat_axis=0, tiled=True)
    sums = jnp.sum(arrived_sums.reshape(owners_total, BINCAP, -1), axis=0)
    own_bins = owner * BINCAP + slot
    own_counts = jnp.sum(
        (own_bins[None, :] == jnp.arange(nbins, dtype=jnp.int32)[:, None]).astype(jnp.float32), axis=1
    )
    arrived_counts = lax.all_to_all(own_counts, "chan", split_axis=0, concat_axis=0, tiled=True)
    counts = jnp.sum(arrived_counts.reshape(owners_total, BINCAP), axis=0)
    return sums / jnp.sqrt(jnp.maximum(counts, 1.0))[:, None]


def solution(mesh):
    return jax.shard_map(
        body,
        mesh=mesh,
        in_specs=(P("win", "chan", None), P(), P("chan", None), P("chan")),
        out_specs=P("chan", "win"),
        check_vma=False,
    )
```

```python
import jax
import jax.numpy as jnp
from jax import lax
from jax.sharding import PartitionSpec as P
from jax.experimental import pallas as pl
from jax.experimental.pallas import tpu as pltpu

LAG = 512
SRC = 2
ROUNDS = 2
BINCAP = 4


block_width = 128


def normalize(traces):
    data = traces.astype(jnp.float32)
    scale = lax.rsqrt(jnp.mean(data * data, axis=-1, keepdims=True) + 1e-06)
    return (data * scale).astype(jnp.bfloat16)


def toeplitz_kernel(src_ref, out_ref):
    for q in range(out_ref.shape[1]):
        row = src_ref[0, q : q + 1, :].astype(jnp.float32)
        row = jnp.concatenate([row, jnp.zeros_like(row)], axis=1)
        band = jnp.broadcast_to(row, (block_width, 2 * block_width))
        out_ref[0, q] = pltpu.roll(band, 0, 1, stride=1, stride_axis=0).astype(out_ref.dtype)


def source_toeplitz(sources):
    n, samples = sources.shape
    quota = samples // block_width
    blocks = sources.reshape(n, quota, block_width)
    return pl.pallas_call(
        toeplitz_kernel,
        grid=(n,),
        in_specs=[pl.BlockSpec((1, quota, block_width), lambda s: (s, 0, 0))],
        out_specs=pl.BlockSpec((1, quota, block_width, 2 * block_width), lambda s: (s, 0, 0, 0)),
        out_shape=jax.ShapeDtypeStruct((n, quota, block_width, 2 * block_width), sources.dtype),
    )(blocks)


def receiver_windows(receivers):
    chans, samples = receivers.shape
    quota = samples // block_width
    lag_blocks = 2 * LAG // block_width
    extended = jnp.pad(receivers, ((0, 0), (LAG, LAG + block_width)))
    cells = extended.reshape(chans, -1, block_width)
    doubled = jnp.concatenate([cells[:, :-1], cells[:, 1:]], axis=-1)
    return jnp.stack([doubled[:, p : p + quota] for p in range(lag_blocks)], axis=1)


def correlate(windows, toeplitz):
    return jnp.einsum("cpqw,sqrw->scpr", windows, toeplitz, preferred_element_type=jnp.float32)


def xor_permute(x, mask, axis, shift, width):
    n = lax.axis_size(axis)

    def moved(step):
        return lambda v: lax.ppermute(v, axis, [(i, i ^ step) for i in range(n)])

    branches = [lambda v: v] + [moved(d << shift) for d in range(1, 1 << width)]
    part = jnp.bitwise_and(jnp.right_shift(mask, shift), (1 << width) - 1)
    return lax.switch(part, branches, x)


def exchange(payload, masks, axis):
    n = lax.axis_size(axis)
    bits = n.bit_length() - 1
    full = n - 1
    first_full = masks[0] == full
    other = jnp.bitwise_xor(jnp.bitwise_xor(masks[0], masks[1]), full)
    fixed = jnp.where(first_full, payload[0], payload[1])
    free = jnp.where(first_full, payload[1], payload[0])
    fixed = lax.ppermute(fixed, axis, [(i, i ^ full) for i in range(n)])
    low = min(bits, 4)
    free = xor_permute(free, other, axis, 0, low)
    if bits > low:
        free = xor_permute(free, other, axis, low, bits - low)
    return jnp.stack(
        [jnp.where(first_full, fixed, free), jnp.where(first_full, free, fixed)]
    )


def body(traces, round_masks, row_owner, row_slot):
    wins, chans, samples = traces.shape
    rows_set = SRC * chans
    normed = normalize(traces)[0]
    stride = chans // SRC
    sources = normed[::stride, :]
    owner = row_owner[:, 0]
    slot = row_slot
    label_rows = []
    for r in range(ROUNDS):
        part = slice((r + 1) * rows_set, (r + 2) * rows_set)
        row = jnp.concatenate([owner[part], slot[part]]).astype(jnp.bfloat16)
        row = jnp.pad(row, (0, samples - row.shape[0]))
        label_rows.append(jnp.concatenate([sources, row[None, :]], axis=0))
    payload = jnp.stack(label_rows)
    arrived = exchange(payload, round_masks, "chan")
    windows = receiver_windows(normed)
    scale = 1.0 / jnp.sqrt(jnp.float32(samples))
    own_band = source_toeplitz(sources)
    chunks = 2
    chunk_windows = [windows[:, h::chunks] for h in range(chunks)]
    own = [correlate(w, own_band) for w in chunk_windows]
    partners = jnp.concatenate([arrived[r, :SRC] for r in range(ROUNDS)], axis=0)
    far_band = source_toeplitz(partners)
    owners_total = lax.axis_size("chan")
    nbins = owners_total * BINCAP
    bins_parts = [owner[:rows_set] * BINCAP + slot[:rows_set]]
    for r in range(ROUNDS):
        got = arrived[r, SRC].astype(jnp.int32)
        bins_parts.append(got[:rows_set] * BINCAP + got[rows_set : 2 * rows_set])
    bins = jnp.concatenate(bins_parts)
    picks = (bins[None, :] == jnp.arange(nbins, dtype=jnp.int32)[:, None]).astype(jnp.float32)
    reduced = []
    for h in range(chunks):
        far = correlate(chunk_windows[h], far_band)
        rows = jnp.concatenate([own[h], far], axis=0) * scale
        rows = rows.reshape(-1, rows.shape[2] * rows.shape[3])
        reduced.append(lax.psum_scatter(rows, "win", scatter_dimension=1, tiled=True))
    parts = []
    for h in range(chunks):
        local = jnp.dot(picks, reduced[h], precision=lax.Precision.HIGHEST, preferred_element_type=jnp.float32)
        arrived_sums = lax.all_to_all(local, "chan", split_axis=0, concat_axis=0, tiled=True)
        parts.append(jnp.sum(arrived_sums.reshape(owners_total, BINCAP, -1), axis=0))
    sums = jnp.concatenate(parts, axis=1)
    own_bins = owner * BINCAP + slot
    own_counts = jnp.sum(
        (own_bins[None, :] == jnp.arange(nbins, dtype=jnp.int32)[:, None]).astype(jnp.float32), axis=1
    )
    arrived_counts = lax.all_to_all(own_counts, "chan", split_axis=0, concat_axis=0, tiled=True)
    counts = jnp.sum(arrived_counts.reshape(owners_total, BINCAP), axis=0)
    return sums / jnp.sqrt(jnp.maximum(counts, 1.0))[:, None]


def solution(mesh):
    return jax.shard_map(
        body,
        mesh=mesh,
        in_specs=(P("win", "chan", None), P(), P("chan", None), P("chan")),
        out_specs=P("chan", "win"),
        check_vma=False,
    )
```

```python
import jax
import jax.numpy as jnp
from jax import lax
from jax.sharding import PartitionSpec as P
from jax.experimental import pallas as pl
from jax.experimental.pallas import tpu as pltpu

LAG = 512
SRC = 2
ROUNDS = 2
BINCAP = 4


block_width = 128


def normalize(traces):
    data = traces.astype(jnp.float32)
    scale = lax.rsqrt(jnp.mean(data * data, axis=-1, keepdims=True) + 1e-06)
    return (data * scale).astype(jnp.bfloat16)


def toeplitz_kernel(src_ref, out_ref):
    for q in range(out_ref.shape[1]):
        row = src_ref[0, q : q + 1, :].astype(jnp.float32)
        row = jnp.concatenate([row, jnp.zeros_like(row)], axis=1)
        band = jnp.broadcast_to(row, (block_width, 2 * block_width))
        out_ref[0, q] = pltpu.roll(band, 0, 1, stride=1, stride_axis=0).astype(out_ref.dtype)


def source_toeplitz(sources):
    n, samples = sources.shape
    quota = samples // block_width
    blocks = sources.reshape(n, quota, block_width)
    return pl.pallas_call(
        toeplitz_kernel,
        grid=(n,),
        in_specs=[pl.BlockSpec((1, quota, block_width), lambda s: (s, 0, 0))],
        out_specs=pl.BlockSpec((1, quota, block_width, 2 * block_width), lambda s: (s, 0, 0, 0)),
        out_shape=jax.ShapeDtypeStruct((n, quota, block_width, 2 * block_width), sources.dtype),
    )(blocks)


def receiver_windows(receivers):
    chans, samples = receivers.shape
    quota = samples // block_width
    lag_blocks = 2 * LAG // block_width
    extended = jnp.pad(receivers, ((0, 0), (LAG, LAG + block_width)))
    cells = extended.reshape(chans, -1, block_width)
    doubled = jnp.concatenate([cells[:, :-1], cells[:, 1:]], axis=-1)
    return jnp.stack([doubled[:, p : p + quota] for p in range(lag_blocks)], axis=1)


def correlate(windows, toeplitz):
    return jnp.einsum("cpqw,sqrw->scpr", windows, toeplitz, preferred_element_type=jnp.float32)


def xor_permute(x, mask, axis, shift, width):
    n = lax.axis_size(axis)

    def moved(step):
        return lambda v: lax.ppermute(v, axis, [(i, i ^ step) for i in range(n)])

    branches = [lambda v: v] + [moved(d << shift) for d in range(1, 1 << width)]
    part = jnp.bitwise_and(jnp.right_shift(mask, shift), (1 << width) - 1)
    return lax.switch(part, branches, x)


def exchange(payload, masks, axis):
    n = lax.axis_size(axis)
    bits = n.bit_length() - 1
    full = n - 1
    first_full = masks[0] == full
    other = jnp.bitwise_xor(jnp.bitwise_xor(masks[0], masks[1]), full)
    fixed = jnp.where(first_full, payload[0], payload[1])
    free = jnp.where(first_full, payload[1], payload[0])
    fixed = lax.ppermute(fixed, axis, [(i, i ^ full) for i in range(n)])
    low = min(bits, 4)
    free = xor_permute(free, other, axis, 0, low)
    if bits > low:
        free = xor_permute(free, other, axis, low, bits - low)
    return jnp.stack(
        [jnp.where(first_full, fixed, free), jnp.where(first_full, free, fixed)]
    )


def body(traces, round_masks, row_owner, row_slot):
    wins, chans, samples = traces.shape
    rows_set = SRC * chans
    normed = normalize(traces)[0]
    stride = chans // SRC
    sources = normed[::stride, :]
    owner = row_owner[:, 0]
    slot = row_slot
    label_rows = []
    for r in range(ROUNDS):
        part = slice((r + 1) * rows_set, (r + 2) * rows_set)
        row = jnp.concatenate([owner[part], slot[part]]).astype(jnp.bfloat16)
        row = jnp.pad(row, (0, samples - row.shape[0]))
        label_rows.append(jnp.concatenate([sources, row[None, :]], axis=0))
    payload = jnp.stack(label_rows)
    arrived = exchange(payload, round_masks, "chan")
    windows = receiver_windows(normed)
    scale = 1.0 / jnp.sqrt(jnp.float32(samples))
    own = correlate(windows, source_toeplitz(sources))
    partners = jnp.concatenate([arrived[r, :SRC] for r in range(ROUNDS)], axis=0)
    far = correlate(windows, source_toeplitz(partners))
    rows = jnp.concatenate([own, far], axis=0) * scale
    rows = rows.reshape(-1, 2 * LAG)
    rows = lax.psum_scatter(rows, "win", scatter_dimension=1, tiled=True)
    owners_total = lax.axis_size("chan")
    nbins = owners_total * BINCAP
    bins_parts = [owner[:rows_set] * BINCAP + slot[:rows_set]]
    for r in range(ROUNDS):
        got = arrived[r, SRC].astype(jnp.int32)
        bins_parts.append(got[:rows_set] * BINCAP + got[rows_set : 2 * rows_set])
    bins = jnp.concatenate(bins_parts)
    picks = (bins[None, :] == jnp.arange(nbins, dtype=jnp.int32)[:, None]).astype(jnp.float32)
    local = jnp.dot(picks, rows, precision=lax.Precision.HIGHEST, preferred_element_type=jnp.float32)
    local = local.reshape(owners_total, BINCAP, -1)
    own_bins = owner * BINCAP + slot
    own_counts = jnp.sum(
        (own_bins[None, :] == jnp.arange(nbins, dtype=jnp.int32)[:, None]).astype(jnp.float32), axis=1
    )
    count_row = jnp.pad(
        own_counts.reshape(owners_total, 1, BINCAP), ((0, 0), (0, 0), (0, local.shape[2] - BINCAP))
    )
    outgoing = jnp.concatenate([local, count_row], axis=1)
    arrived_sums = lax.all_to_all(outgoing, "chan", split_axis=0, concat_axis=0, tiled=True)
    arrived_sums = jnp.sum(arrived_sums, axis=0)
    sums = arrived_sums[:BINCAP]
    counts = arrived_sums[BINCAP, :BINCAP]
    return sums / jnp.sqrt(jnp.maximum(counts, 1.0))[:, None]


def solution(mesh):
    return jax.shard_map(
        body,
        mesh=mesh,
        in_specs=(P("win", "chan", None), P(), P("chan", None), P("chan")),
        out_specs=P("chan", "win"),
        check_vma=False,
    )
```

```python
import jax
import jax.numpy as jnp
from jax import lax
from jax.sharding import PartitionSpec as P
from jax.experimental import pallas as pl
from jax.experimental.pallas import tpu as pltpu

LAG = 512
SRC = 2
ROUNDS = 2
BINCAP = 4


block_width = 128


def normalize(traces):
    data = traces.astype(jnp.float32)
    scale = lax.rsqrt(jnp.mean(data * data, axis=-1, keepdims=True) + 1e-06)
    return (data * scale).astype(jnp.bfloat16)


def toeplitz_kernel(src_ref, out_ref):
    for q in range(out_ref.shape[1]):
        row = src_ref[0, q : q + 1, :].astype(jnp.float32)
        row = jnp.concatenate([row, jnp.zeros_like(row)], axis=1)
        band = jnp.broadcast_to(row, (block_width, 2 * block_width))
        out_ref[0, q] = pltpu.roll(band, 0, 1, stride=1, stride_axis=0).astype(out_ref.dtype)


def source_toeplitz(sources):
    n, samples = sources.shape
    quota = samples // block_width
    blocks = sources.reshape(n, quota, block_width)
    return pl.pallas_call(
        toeplitz_kernel,
        grid=(n,),
        in_specs=[pl.BlockSpec((1, quota, block_width), lambda s: (s, 0, 0))],
        out_specs=pl.BlockSpec((1, quota, block_width, 2 * block_width), lambda s: (s, 0, 0, 0)),
        out_shape=jax.ShapeDtypeStruct((n, quota, block_width, 2 * block_width), sources.dtype),
    )(blocks)


def receiver_windows(receivers):
    chans, samples = receivers.shape
    quota = samples // block_width
    lag_blocks = 2 * LAG // block_width
    extended = jnp.pad(receivers, ((0, 0), (LAG, LAG + block_width)))
    cells = extended.reshape(chans, -1, block_width)
    doubled = jnp.concatenate([cells[:, :-1], cells[:, 1:]], axis=-1)
    return jnp.stack([doubled[:, p : p + quota] for p in range(lag_blocks)], axis=1)


def correlate(windows, toeplitz):
    return jnp.einsum("cpqw,sqrw->scpr", windows, toeplitz, preferred_element_type=jnp.float32)


def xor_permute(x, mask, axis, shift, width):
    n = lax.axis_size(axis)

    def moved(step):
        return lambda v: lax.ppermute(v, axis, [(i, i ^ step) for i in range(n)])

    branches = [lambda v: v] + [moved(d << shift) for d in range(1, 1 << width)]
    part = jnp.bitwise_and(jnp.right_shift(mask, shift), (1 << width) - 1)
    return lax.switch(part, branches, x)


def exchange(payload, masks, axis):
    n = lax.axis_size(axis)
    bits = n.bit_length() - 1
    full = n - 1
    first_full = masks[0] == full
    other = jnp.bitwise_xor(jnp.bitwise_xor(masks[0], masks[1]), full)
    fixed = jnp.where(first_full, payload[0], payload[1])
    free = jnp.where(first_full, payload[1], payload[0])
    fixed = lax.ppermute(fixed, axis, [(i, i ^ full) for i in range(n)])
    low = min(bits, 4)
    free = xor_permute(free, other, axis, 0, low)
    if bits > low:
        free = xor_permute(free, other, axis, low, bits - low)
    return jnp.stack(
        [jnp.where(first_full, fixed, free), jnp.where(first_full, free, fixed)]
    )


def body(traces, round_masks, row_owner, row_slot):
    wins, chans, samples = traces.shape
    rows_set = SRC * chans
    normed = normalize(traces)[0]
    stride = chans // SRC
    sources = normed[::stride, :]
    owner = row_owner[:, 0]
    slot = row_slot
    label_rows = []
    for r in range(ROUNDS):
        part = slice((r + 1) * rows_set, (r + 2) * rows_set)
        row = jnp.concatenate([owner[part], slot[part]]).astype(jnp.bfloat16)
        row = jnp.pad(row, (0, samples - row.shape[0]))
        label_rows.append(jnp.concatenate([sources, row[None, :]], axis=0))
    payload = jnp.stack(label_rows)
    windows = receiver_windows(normed)
    scale = 1.0 / jnp.sqrt(jnp.float32(samples))
    own = correlate(windows, source_toeplitz(sources))
    own, payload = lax.optimization_barrier((own, payload))
    arrived = exchange(payload, round_masks, "chan")
    partners = jnp.concatenate([arrived[r, :SRC] for r in range(ROUNDS)], axis=0)
    far = correlate(windows, source_toeplitz(partners))
    rows = jnp.concatenate([own, far], axis=0) * scale
    rows = rows.reshape(-1, 2 * LAG)
    rows = lax.psum_scatter(rows, "win", scatter_dimension=1, tiled=True)
    owners_total = lax.axis_size("chan")
    nbins = owners_total * BINCAP
    bins_parts = [owner[:rows_set] * BINCAP + slot[:rows_set]]
    for r in range(ROUNDS):
        got = arrived[r, SRC].astype(jnp.int32)
        bins_parts.append(got[:rows_set] * BINCAP + got[rows_set : 2 * rows_set])
    bins = jnp.concatenate(bins_parts)
    picks = (bins[None, :] == jnp.arange(nbins, dtype=jnp.int32)[:, None]).astype(jnp.float32)
    local = jnp.dot(picks, rows, precision=lax.Precision.HIGHEST, preferred_element_type=jnp.float32)
    arrived_sums = lax.all_to_all(local, "chan", split_axis=0, concat_axis=0, tiled=True)
    sums = jnp.sum(arrived_sums.reshape(owners_total, BINCAP, -1), axis=0)
    own_bins = owner * BINCAP + slot
    own_counts = jnp.sum(
        (own_bins[None, :] == jnp.arange(nbins, dtype=jnp.int32)[:, None]).astype(jnp.float32), axis=1
    )
    arrived_counts = lax.all_to_all(own_counts, "chan", split_axis=0, concat_axis=0, tiled=True)
    counts = jnp.sum(arrived_counts.reshape(owners_total, BINCAP), axis=0)
    return sums / jnp.sqrt(jnp.maximum(counts, 1.0))[:, None]


def solution(mesh):
    return jax.shard_map(
        body,
        mesh=mesh,
        in_specs=(P("win", "chan", None), P(), P("chan", None), P("chan")),
        out_specs=P("chan", "win"),
        check_vma=False,
    )
```

```python
import jax
import jax.numpy as jnp
from jax import lax
from jax.sharding import PartitionSpec as P
from jax.experimental import pallas as pl
from jax.experimental.pallas import tpu as pltpu

LAG = 512
SRC = 2
ROUNDS = 2
BINCAP = 4


block_width = 128


def normalize(traces):
    data = traces.astype(jnp.float32)
    scale = lax.rsqrt(jnp.mean(data * data, axis=-1, keepdims=True) + 1e-06)
    return (data * scale).astype(jnp.bfloat16)


def toeplitz_kernel(src_ref, out_ref):
    for q in range(out_ref.shape[1]):
        row = src_ref[0, q : q + 1, :].astype(jnp.float32)
        row = jnp.concatenate([row, jnp.zeros_like(row)], axis=1)
        band = jnp.broadcast_to(row, (block_width, 2 * block_width))
        out_ref[0, q] = pltpu.roll(band, 0, 1, stride=1, stride_axis=0).astype(out_ref.dtype)


def source_toeplitz(sources):
    n, samples = sources.shape
    quota = samples // block_width
    blocks = sources.reshape(n, quota, block_width)
    return pl.pallas_call(
        toeplitz_kernel,
        grid=(n,),
        in_specs=[pl.BlockSpec((1, quota, block_width), lambda s: (s, 0, 0))],
        out_specs=pl.BlockSpec((1, quota, block_width, 2 * block_width), lambda s: (s, 0, 0, 0)),
        out_shape=jax.ShapeDtypeStruct((n, quota, block_width, 2 * block_width), sources.dtype),
    )(blocks)


def receiver_windows(receivers):
    chans, samples = receivers.shape
    quota = samples // block_width
    lag_blocks = 2 * LAG // block_width
    extended = jnp.pad(receivers, ((0, 0), (LAG, LAG + block_width)))
    cells = extended.reshape(chans, -1, block_width)
    doubled = jnp.concatenate([cells[:, :-1], cells[:, 1:]], axis=-1)
    return jnp.stack([doubled[:, p : p + quota] for p in range(lag_blocks)], axis=1)


def correlate(windows, toeplitz):
    return jnp.einsum("cpqw,sqrw->scpr", windows, toeplitz, preferred_element_type=jnp.float32)


def xor_level(fixed, free, mask, full, axis, shift, width):
    n = lax.axis_size(axis)
    span = (1 << width) - 1
    fixed_step = ((full >> shift) & span) << shift

    def moved(step):
        def go(pair):
            fixed_part, free_part = pair
            fixed_part = lax.ppermute(fixed_part, axis, [(i, i ^ fixed_step) for i in range(n)])
            if step:
                free_part = lax.ppermute(free_part, axis, [(i, i ^ step) for i in range(n)])
            return fixed_part, free_part

        return go

    part = jnp.bitwise_and(jnp.right_shift(mask, shift), span)
    return lax.switch(part, [moved(d << shift) for d in range(1 << width)], (fixed, free))


def exchange(payload, masks, axis):
    n = lax.axis_size(axis)
    bits = n.bit_length() - 1
    full = n - 1
    first_full = masks[0] == full
    other = jnp.bitwise_xor(jnp.bitwise_xor(masks[0], masks[1]), full)
    fixed = jnp.where(first_full, payload[0], payload[1])
    free = jnp.where(first_full, payload[1], payload[0])
    low = min(bits, 4)
    fixed, free = xor_level(fixed, free, other, full, axis, 0, low)
    if bits > low:
        fixed, free = xor_level(fixed, free, other, full, axis, low, bits - low)
    return jnp.stack(
        [jnp.where(first_full, fixed, free), jnp.where(first_full, free, fixed)]
    )


def body(traces, round_masks, row_owner, row_slot):
    wins, chans, samples = traces.shape
    rows_set = SRC * chans
    normed = normalize(traces)[0]
    stride = chans // SRC
    sources = normed[::stride, :]
    owner = row_owner[:, 0]
    slot = row_slot
    label_rows = []
    for r in range(ROUNDS):
        part = slice((r + 1) * rows_set, (r + 2) * rows_set)
        row = jnp.concatenate([owner[part], slot[part]]).astype(jnp.bfloat16)
        row = jnp.pad(row, (0, samples - row.shape[0]))
        label_rows.append(jnp.concatenate([sources, row[None, :]], axis=0))
    payload = jnp.stack(label_rows)
    arrived = exchange(payload, round_masks, "chan")
    windows = receiver_windows(normed)
    scale = 1.0 / jnp.sqrt(jnp.float32(samples))
    own = correlate(windows, source_toeplitz(sources))
    partners = jnp.concatenate([arrived[r, :SRC] for r in range(ROUNDS)], axis=0)
    far = correlate(windows, source_toeplitz(partners))
    rows = jnp.concatenate([own, far], axis=0) * scale
    rows = rows.reshape(-1, 2 * LAG)
    rows = lax.psum_scatter(rows, "win", scatter_dimension=1, tiled=True)
    owners_total = lax.axis_size("chan")
    nbins = owners_total * BINCAP
    bins_parts = [owner[:rows_set] * BINCAP + slot[:rows_set]]
    for r in range(ROUNDS):
        got = arrived[r, SRC].astype(jnp.int32)
        bins_parts.append(got[:rows_set] * BINCAP + got[rows_set : 2 * rows_set])
    bins = jnp.concatenate(bins_parts)
    picks = (bins[None, :] == jnp.arange(nbins, dtype=jnp.int32)[:, None]).astype(jnp.float32)
    local = jnp.dot(picks, rows, precision=lax.Precision.HIGHEST, preferred_element_type=jnp.float32)
    arrived_sums = lax.all_to_all(local, "chan", split_axis=0, concat_axis=0, tiled=True)
    sums = jnp.sum(arrived_sums.reshape(owners_total, BINCAP, -1), axis=0)
    own_bins = owner * BINCAP + slot
    own_counts = jnp.sum(
        (own_bins[None, :] == jnp.arange(nbins, dtype=jnp.int32)[:, None]).astype(jnp.float32), axis=1
    )
    arrived_counts = lax.all_to_all(own_counts, "chan", split_axis=0, concat_axis=0, tiled=True)
    counts = jnp.sum(arrived_counts.reshape(owners_total, BINCAP), axis=0)
    return sums / jnp.sqrt(jnp.maximum(counts, 1.0))[:, None]


def solution(mesh):
    return jax.shard_map(
        body,
        mesh=mesh,
        in_specs=(P("win", "chan", None), P(), P("chan", None), P("chan")),
        out_specs=P("chan", "win"),
        check_vma=False,
    )
```

```python
import jax
import jax.numpy as jnp
from jax import lax
from jax.sharding import PartitionSpec as P
from jax.experimental import pallas as pl
from jax.experimental.pallas import tpu as pltpu

LAG = 512
SRC = 2
ROUNDS = 2
BINCAP = 4


block_width = 128


def normalize(traces):
    data = traces.astype(jnp.float32)
    scale = lax.rsqrt(jnp.mean(data * data, axis=-1, keepdims=True) + 1e-06)
    return (data * scale).astype(jnp.bfloat16)


def toeplitz_kernel(src_ref, out_ref):
    for q in range(out_ref.shape[1]):
        row = src_ref[0, q : q + 1, :].astype(jnp.float32)
        row = jnp.concatenate([row, jnp.zeros_like(row)], axis=1)
        band = jnp.broadcast_to(row, (block_width, 2 * block_width))
        out_ref[0, q] = pltpu.roll(band, 0, 1, stride=1, stride_axis=0).astype(out_ref.dtype)


def source_toeplitz(sources):
    n, samples = sources.shape
    quota = samples // block_width
    blocks = sources.reshape(n, quota, block_width)
    return pl.pallas_call(
        toeplitz_kernel,
        grid=(n,),
        in_specs=[pl.BlockSpec((1, quota, block_width), lambda s: (s, 0, 0))],
        out_specs=pl.BlockSpec((1, quota, block_width, 2 * block_width), lambda s: (s, 0, 0, 0)),
        out_shape=jax.ShapeDtypeStruct((n, quota, block_width, 2 * block_width), sources.dtype),
    )(blocks)


def receiver_windows(receivers):
    chans, samples = receivers.shape
    quota = samples // block_width
    lag_blocks = 2 * LAG // block_width
    extended = jnp.pad(receivers, ((0, 0), (LAG, LAG + block_width)))
    cells = extended.reshape(chans, -1, block_width)
    doubled = jnp.concatenate([cells[:, :-1], cells[:, 1:]], axis=-1)
    return jnp.stack([doubled[:, p : p + quota] for p in range(lag_blocks)], axis=1)


def correlate(windows, toeplitz):
    return jnp.einsum("cpqw,sqrw->scpr", windows, toeplitz, preferred_element_type=jnp.float32)


def xor_permute(x, mask, axis, shift, width):
    n = lax.axis_size(axis)

    def moved(step):
        return lambda v: lax.ppermute(v, axis, [(i, i ^ step) for i in range(n)])

    branches = [lambda v: v] + [moved(d << shift) for d in range(1, 1 << width)]
    part = jnp.bitwise_and(jnp.right_shift(mask, shift), (1 << width) - 1)
    return lax.switch(part, branches, x)


def exchange(payload, masks, axis):
    n = lax.axis_size(axis)
    bits = n.bit_length() - 1
    full = n - 1
    first_full = masks[0] == full
    other = jnp.bitwise_xor(jnp.bitwise_xor(masks[0], masks[1]), full)
    fixed = jnp.where(first_full, payload[0], payload[1])
    free = jnp.where(first_full, payload[1], payload[0])
    fixed = lax.ppermute(fixed, axis, [(i, i ^ full) for i in range(n)])
    low = min(bits, 4)
    free = xor_permute(free, other, axis, 0, low)
    if bits > low:
        free = xor_permute(free, other, axis, low, bits - low)
    return jnp.stack(
        [jnp.where(first_full, fixed, free), jnp.where(first_full, free, fixed)]
    )


def body(traces, round_masks, row_owner, row_slot):
    wins, chans, samples = traces.shape
    rows_set = SRC * chans
    normed = normalize(traces)[0]
    stride = chans // SRC
    sources = normed[::stride, :]
    owner = row_owner[:, 0]
    slot = row_slot
    label_rows = []
    for r in range(ROUNDS):
        part = slice((r + 1) * rows_set, (r + 2) * rows_set)
        row = jnp.concatenate([owner[part], slot[part]]).astype(jnp.bfloat16)
        row = jnp.pad(row, (0, samples - row.shape[0]))
        label_rows.append(jnp.concatenate([sources, row[None, :]], axis=0))
    payload = jnp.stack(label_rows)
    arrived = exchange(payload, round_masks, "chan")
    windows = receiver_windows(normed)
    scale = 1.0 / jnp.sqrt(jnp.float32(samples))
    own = correlate(windows, source_toeplitz(sources))
    partners = jnp.concatenate([arrived[r, :SRC] for r in range(ROUNDS)], axis=0)
    far = correlate(windows, source_toeplitz(partners))
    rows = jnp.concatenate([own, far], axis=0) * scale
    rows = rows.reshape(-1, 2 * LAG)
    wins_total = lax.axis_size("win")
    rows = rows.reshape(rows.shape[0], wins_total, -1)
    rows = jnp.sum(lax.all_to_all(rows, "win", split_axis=1, concat_axis=1, tiled=True), axis=1)
    owners_total = lax.axis_size("chan")
    nbins = owners_total * BINCAP
    bins_parts = [owner[:rows_set] * BINCAP + slot[:rows_set]]
    for r in range(ROUNDS):
        got = arrived[r, SRC].astype(jnp.int32)
        bins_parts.append(got[:rows_set] * BINCAP + got[rows_set : 2 * rows_set])
    bins = jnp.concatenate(bins_parts)
    picks = (bins[None, :] == jnp.arange(nbins, dtype=jnp.int32)[:, None]).astype(jnp.float32)
    local = jnp.dot(picks, rows, precision=lax.Precision.HIGHEST, preferred_element_type=jnp.float32)
    arrived_sums = lax.all_to_all(local, "chan", split_axis=0, concat_axis=0, tiled=True)
    sums = jnp.sum(arrived_sums.reshape(owners_total, BINCAP, -1), axis=0)
    own_bins = owner * BINCAP + slot
    own_counts = jnp.sum(
        (own_bins[None, :] == jnp.arange(nbins, dtype=jnp.int32)[:, None]).astype(jnp.float32), axis=1
    )
    arrived_counts = lax.all_to_all(own_counts, "chan", split_axis=0, concat_axis=0, tiled=True)
    counts = jnp.sum(arrived_counts.reshape(owners_total, BINCAP), axis=0)
    return sums / jnp.sqrt(jnp.maximum(counts, 1.0))[:, None]


def solution(mesh):
    return jax.shard_map(
        body,
        mesh=mesh,
        in_specs=(P("win", "chan", None), P(), P("chan", None), P("chan")),
        out_specs=P("chan", "win"),
        check_vma=False,
    )
```

```python
import jax
import jax.numpy as jnp
from jax import lax
from jax.sharding import PartitionSpec as P
from jax.experimental import pallas as pl
from jax.experimental.pallas import tpu as pltpu

LAG = 512
SRC = 2
ROUNDS = 2
BINCAP = 4


block_width = 128


def normalize(traces):
    data = traces.astype(jnp.float32)
    scale = lax.rsqrt(jnp.mean(data * data, axis=-1, keepdims=True) + 1e-06)
    return (data * scale).astype(jnp.bfloat16)


def toeplitz_kernel(src_ref, out_ref):
    for q in range(out_ref.shape[1]):
        row = src_ref[0, q : q + 1, :].astype(jnp.float32)
        row = jnp.concatenate([row, jnp.zeros_like(row)], axis=1)
        band = jnp.broadcast_to(row, (block_width, 2 * block_width))
        out_ref[0, q] = pltpu.roll(band, 0, 1, stride=1, stride_axis=0).astype(out_ref.dtype)


def source_toeplitz(sources):
    n, samples = sources.shape
    quota = samples // block_width
    blocks = sources.reshape(n, quota, block_width)
    return pl.pallas_call(
        toeplitz_kernel,
        grid=(n,),
        in_specs=[pl.BlockSpec((1, quota, block_width), lambda s: (s, 0, 0))],
        out_specs=pl.BlockSpec((1, quota, block_width, 2 * block_width), lambda s: (s, 0, 0, 0)),
        out_shape=jax.ShapeDtypeStruct((n, quota, block_width, 2 * block_width), sources.dtype),
    )(blocks)


def receiver_windows(receivers):
    chans, samples = receivers.shape
    quota = samples // block_width
    lag_blocks = 2 * LAG // block_width
    extended = jnp.pad(receivers, ((0, 0), (LAG, LAG + block_width)))
    cells = extended.reshape(chans, -1, block_width)
    doubled = jnp.concatenate([cells[:, :-1], cells[:, 1:]], axis=-1)
    return jnp.stack([doubled[:, p : p + quota] for p in range(lag_blocks)], axis=1)


def correlate(windows, toeplitz):
    return jnp.einsum("cpqw,sqrw->scpr", windows, toeplitz, preferred_element_type=jnp.float32)


def xor_permute(x, mask, axis, shift, width):
    n = lax.axis_size(axis)

    def moved(step):
        return lambda v: lax.ppermute(v, axis, [(i, i ^ step) for i in range(n)])

    branches = [lambda v: v] + [moved(d << shift) for d in range(1, 1 << width)]
    part = jnp.bitwise_and(jnp.right_shift(mask, shift), (1 << width) - 1)
    return lax.switch(part, branches, x)


def exchange(payload, masks, axis):
    n = lax.axis_size(axis)
    bits = n.bit_length() - 1
    full = n - 1
    first_full = masks[0] == full
    other = jnp.bitwise_xor(jnp.bitwise_xor(masks[0], masks[1]), full)
    fixed = jnp.where(first_full, payload[0], payload[1])
    free = jnp.where(first_full, payload[1], payload[0])
    fixed = lax.ppermute(fixed, axis, [(i, i ^ full) for i in range(n)])
    low = min(bits, 4)
    free = xor_permute(free, other, axis, 0, low)
    if bits > low:
        free = xor_permute(free, other, axis, low, bits - low)
    return jnp.stack(
        [jnp.where(first_full, fixed, free), jnp.where(first_full, free, fixed)]
    )


def body(traces, round_masks, row_owner, row_slot):
    wins, chans, samples = traces.shape
    rows_set = SRC * chans
    normed = normalize(traces)[0]
    stride = chans // SRC
    sources = normed[::stride, :]
    owner = row_owner[:, 0]
    slot = row_slot
    label_rows = []
    for r in range(ROUNDS):
        part = slice((r + 1) * rows_set, (r + 2) * rows_set)
        row = jnp.concatenate([owner[part], slot[part]]).astype(jnp.bfloat16)
        row = jnp.pad(row, (0, samples - row.shape[0]))
        label_rows.append(jnp.concatenate([sources, row[None, :]], axis=0))
    payload = jnp.stack(label_rows)
    arrived = exchange(payload, round_masks, "chan")
    windows = receiver_windows(normed)
    scale = 1.0 / jnp.sqrt(jnp.float32(samples))
    own = correlate(windows, source_toeplitz(sources))
    partners = jnp.concatenate([arrived[r, :SRC] for r in range(ROUNDS)], axis=0)
    far = correlate(windows, source_toeplitz(partners))
    rows = jnp.concatenate([own, far], axis=0) * scale
    rows = rows.reshape(-1, 2 * LAG)
    wins_total = lax.axis_size("win")
    rows = rows.reshape(rows.shape[0], wins_total, -1)
    rows = jnp.sum(lax.all_to_all(rows, "win", split_axis=1, concat_axis=1, tiled=True), axis=1)
    owners_total = lax.axis_size("chan")
    nbins = owners_total * BINCAP
    bins_parts = [owner[:rows_set] * BINCAP + slot[:rows_set]]
    for r in range(ROUNDS):
        got = arrived[r, SRC].astype(jnp.int32)
        bins_parts.append(got[:rows_set] * BINCAP + got[rows_set : 2 * rows_set])
    bins = jnp.concatenate(bins_parts)
    picks = (bins[None, :] == jnp.arange(nbins, dtype=jnp.int32)[:, None]).astype(jnp.float32)
    local = jnp.dot(picks, rows, precision=lax.Precision.HIGHEST, preferred_element_type=jnp.float32)
    own_bins = owner * BINCAP + slot
    own_counts = jnp.sum(
        (own_bins[None, :] == jnp.arange(nbins, dtype=jnp.int32)[:, None]).astype(jnp.float32), axis=1
    )
    local = local.reshape(owners_total, BINCAP, -1)
    count_cols = jnp.broadcast_to(own_counts.reshape(owners_total, BINCAP, 1), (owners_total, BINCAP, block_width))
    outgoing = jnp.concatenate([local, count_cols], axis=2)
    arrived_sums = jnp.sum(lax.all_to_all(outgoing, "chan", split_axis=0, concat_axis=0, tiled=True), axis=0)
    sums = arrived_sums[:, : local.shape[2]]
    counts = arrived_sums[:, local.shape[2]]
    return sums / jnp.sqrt(jnp.maximum(counts, 1.0))[:, None]


def solution(mesh):
    return jax.shard_map(
        body,
        mesh=mesh,
        in_specs=(P("win", "chan", None), P(), P("chan", None), P("chan")),
        out_specs=P("chan", "win"),
        check_vma=False,
    )
```

```python
import jax
import jax.numpy as jnp
from jax import lax
from jax.sharding import PartitionSpec as P
from jax.experimental import pallas as pl
from jax.experimental.pallas import tpu as pltpu

LAG = 512
SRC = 2
ROUNDS = 2
BINCAP = 4


block_width = 128


def normalize(traces):
    data = traces.astype(jnp.float32)
    scale = lax.rsqrt(jnp.mean(data * data, axis=-1, keepdims=True) + 1e-06)
    return (data * scale).astype(jnp.bfloat16)


def toeplitz_kernel(src_ref, out_ref):
    for q in range(out_ref.shape[1]):
        row = src_ref[0, q : q + 1, :].astype(jnp.float32)
        row = jnp.concatenate([row, jnp.zeros_like(row)], axis=1)
        band = jnp.broadcast_to(row, (block_width, 2 * block_width))
        out_ref[0, q] = pltpu.roll(band, 0, 1, stride=1, stride_axis=0).astype(out_ref.dtype)


def source_toeplitz(sources):
    n, samples = sources.shape
    quota = samples // block_width
    blocks = sources.reshape(n, quota, block_width)
    return pl.pallas_call(
        toeplitz_kernel,
        grid=(n,),
        in_specs=[pl.BlockSpec((1, quota, block_width), lambda s: (s, 0, 0))],
        out_specs=pl.BlockSpec((1, quota, block_width, 2 * block_width), lambda s: (s, 0, 0, 0)),
        out_shape=jax.ShapeDtypeStruct((n, quota, block_width, 2 * block_width), sources.dtype),
    )(blocks)


def receiver_windows(receivers):
    chans, samples = receivers.shape
    quota = samples // block_width
    lag_blocks = 2 * LAG // block_width
    extended = jnp.pad(receivers, ((0, 0), (LAG, LAG + block_width)))
    cells = extended.reshape(chans, -1, block_width)
    doubled = jnp.concatenate([cells[:, :-1], cells[:, 1:]], axis=-1)
    return jnp.stack([doubled[:, p : p + quota] for p in range(lag_blocks)], axis=1)


def correlate(windows, toeplitz):
    return jnp.einsum("cpqw,sqrw->scpr", windows, toeplitz, preferred_element_type=jnp.float32)


def xor_permute(x, mask, axis, shift, width):
    n = lax.axis_size(axis)

    def moved(step):
        return lambda v: lax.ppermute(v, axis, [(i, i ^ step) for i in range(n)])

    branches = [lambda v: v] + [moved(d << shift) for d in range(1, 1 << width)]
    part = jnp.bitwise_and(jnp.right_shift(mask, shift), (1 << width) - 1)
    return lax.switch(part, branches, x)


def exchange(payload, masks, axis):
    n = lax.axis_size(axis)
    bits = n.bit_length() - 1
    full = n - 1
    first_full = masks[0] == full
    other = jnp.bitwise_xor(jnp.bitwise_xor(masks[0], masks[1]), full)
    fixed = jnp.where(first_full, payload[0], payload[1])
    free = jnp.where(first_full, payload[1], payload[0])
    fixed = lax.ppermute(fixed, axis, [(i, i ^ full) for i in range(n)])
    low = min(bits, 4)
    free = xor_permute(free, other, axis, 0, low)
    if bits > low:
        free = xor_permute(free, other, axis, low, bits - low)
    return jnp.stack(
        [jnp.where(first_full, fixed, free), jnp.where(first_full, free, fixed)]
    )


def body(traces, round_masks, row_owner, row_slot):
    wins, chans, samples = traces.shape
    rows_set = SRC * chans
    normed = normalize(traces)[0]
    stride = chans // SRC
    sources = normed[::stride, :]
    owner = row_owner[:, 0]
    slot = row_slot
    label_rows = []
    for r in range(ROUNDS):
        part = slice((r + 1) * rows_set, (r + 2) * rows_set)
        row = jnp.concatenate([owner[part], slot[part]]).astype(jnp.bfloat16)
        row = jnp.pad(row, (0, samples - row.shape[0]))
        label_rows.append(jnp.concatenate([sources, row[None, :]], axis=0))
    payload = jnp.stack(label_rows)
    arrived = exchange(payload, round_masks, "chan")
    windows = receiver_windows(normed)
    scale = 1.0 / jnp.sqrt(jnp.float32(samples))
    own = correlate(windows, source_toeplitz(sources))
    partners = jnp.concatenate([arrived[r, :SRC] for r in range(ROUNDS)], axis=0)
    far = correlate(windows, source_toeplitz(partners))
    rows = jnp.concatenate([own, far], axis=0) * scale
    rows = rows.reshape(-1, 2 * LAG)
    wins_total = lax.axis_size("win")
    rows = rows.reshape(rows.shape[0], wins_total, -1)
    rows = lax.all_to_all(rows.astype(jnp.bfloat16), "win", split_axis=1, concat_axis=1, tiled=True)
    rows = jnp.sum(rows.astype(jnp.float32), axis=1)
    owners_total = lax.axis_size("chan")
    nbins = owners_total * BINCAP
    bins_parts = [owner[:rows_set] * BINCAP + slot[:rows_set]]
    for r in range(ROUNDS):
        got = arrived[r, SRC].astype(jnp.int32)
        bins_parts.append(got[:rows_set] * BINCAP + got[rows_set : 2 * rows_set])
    bins = jnp.concatenate(bins_parts)
    picks = (bins[None, :] == jnp.arange(nbins, dtype=jnp.int32)[:, None]).astype(jnp.float32)
    local = jnp.dot(picks, rows, precision=lax.Precision.HIGHEST, preferred_element_type=jnp.float32)
    own_bins = owner * BINCAP + slot
    own_counts = jnp.sum(
        (own_bins[None, :] == jnp.arange(nbins, dtype=jnp.int32)[:, None]).astype(jnp.float32), axis=1
    )
    local = local.reshape(owners_total, BINCAP, -1)
    count_cols = jnp.broadcast_to(own_counts.reshape(owners_total, BINCAP, 1), (owners_total, BINCAP, block_width))
    outgoing = jnp.concatenate([local, count_cols], axis=2)
    arrived_sums = lax.all_to_all(outgoing.astype(jnp.bfloat16), "chan", split_axis=0, concat_axis=0, tiled=True)
    arrived_sums = jnp.sum(arrived_sums.astype(jnp.float32), axis=0)
    sums = arrived_sums[:, : local.shape[2]]
    counts = arrived_sums[:, local.shape[2]]
    return sums / jnp.sqrt(jnp.maximum(counts, 1.0))[:, None]


def solution(mesh):
    return jax.shard_map(
        body,
        mesh=mesh,
        in_specs=(P("win", "chan", None), P(), P("chan", None), P("chan")),
        out_specs=P("chan", "win"),
        check_vma=False,
    )
```

```python
import jax
import jax.numpy as jnp
from jax import lax
from jax.sharding import PartitionSpec as P
from jax.experimental import pallas as pl
from jax.experimental.pallas import tpu as pltpu

LAG = 512
SRC = 2
ROUNDS = 2
BINCAP = 4


block_width = 128


def normalize(traces):
    data = traces.astype(jnp.float32)
    scale = lax.rsqrt(jnp.mean(data * data, axis=-1, keepdims=True) + 1e-06)
    return (data * scale).astype(jnp.bfloat16)


def toeplitz_kernel(src_ref, out_ref):
    for q in range(out_ref.shape[1]):
        row = src_ref[0, q : q + 1, :].astype(jnp.float32)
        row = jnp.concatenate([row, jnp.zeros_like(row)], axis=1)
        band = jnp.broadcast_to(row, (block_width, 2 * block_width))
        out_ref[0, q] = pltpu.roll(band, 0, 1, stride=1, stride_axis=0).astype(out_ref.dtype)


def source_toeplitz(sources):
    n, samples = sources.shape
    quota = samples // block_width
    blocks = sources.reshape(n, quota, block_width)
    return pl.pallas_call(
        toeplitz_kernel,
        grid=(n,),
        in_specs=[pl.BlockSpec((1, quota, block_width), lambda s: (s, 0, 0))],
        out_specs=pl.BlockSpec((1, quota, block_width, 2 * block_width), lambda s: (s, 0, 0, 0)),
        out_shape=jax.ShapeDtypeStruct((n, quota, block_width, 2 * block_width), sources.dtype),
    )(blocks)


def receiver_windows(receivers):
    chans, samples = receivers.shape
    quota = samples // block_width
    lag_blocks = 2 * LAG // block_width
    extended = jnp.pad(receivers, ((0, 0), (LAG, LAG + block_width)))
    cells = extended.reshape(chans, -1, block_width)
    doubled = jnp.concatenate([cells[:, :-1], cells[:, 1:]], axis=-1)
    return jnp.stack([doubled[:, p : p + quota] for p in range(lag_blocks)], axis=1)


def correlate(windows, toeplitz):
    return jnp.einsum("cpqw,sqrw->scpr", windows, toeplitz, preferred_element_type=jnp.float32)


def xor_permute(x, mask, axis, shift, width):
    n = lax.axis_size(axis)

    def moved(step):
        return lambda v: lax.ppermute(v, axis, [(i, i ^ step) for i in range(n)])

    branches = [lambda v: v] + [moved(d << shift) for d in range(1, 1 << width)]
    part = jnp.bitwise_and(jnp.right_shift(mask, shift), (1 << width) - 1)
    return lax.switch(part, branches, x)


def exchange(payload, masks, axis):
    n = lax.axis_size(axis)
    bits = n.bit_length() - 1
    full = n - 1
    first_full = masks[0] == full
    other = jnp.bitwise_xor(jnp.bitwise_xor(masks[0], masks[1]), full)
    fixed = jnp.where(first_full, payload[0], payload[1])
    free = jnp.where(first_full, payload[1], payload[0])
    fixed = lax.ppermute(fixed, axis, [(i, i ^ full) for i in range(n)])
    low = min(bits, 4)
    free = xor_permute(free, other, axis, 0, low)
    if bits > low:
        free = xor_permute(free, other, axis, low, bits - low)
    return jnp.stack(
        [jnp.where(first_full, fixed, free), jnp.where(first_full, free, fixed)]
    )


def body(traces, round_masks, row_owner, row_slot):
    wins, chans, samples = traces.shape
    rows_set = SRC * chans
    normed = normalize(traces)[0]
    stride = chans // SRC
    sources = normed[::stride, :]
    owner = row_owner[:, 0]
    slot = row_slot
    label_rows = []
    for r in range(ROUNDS):
        part = slice((r + 1) * rows_set, (r + 2) * rows_set)
        row = jnp.concatenate([owner[part], slot[part]]).astype(jnp.bfloat16)
        row = jnp.pad(row, (0, samples - row.shape[0]))
        label_rows.append(jnp.concatenate([sources, row[None, :]], axis=0))
    payload = jnp.stack(label_rows)
    arrived = exchange(payload, round_masks, "chan")
    windows = receiver_windows(normed)
    scale = 1.0 / jnp.sqrt(jnp.float32(samples))
    wins_total = lax.axis_size("win")

    def window_sum(part):
        part = (part * scale).reshape(-1, wins_total, 2 * LAG // wins_total)
        part = lax.all_to_all(part.astype(jnp.bfloat16), "win", split_axis=1, concat_axis=1, tiled=True)
        return jnp.sum(part.astype(jnp.float32), axis=1)

    own = window_sum(correlate(windows, source_toeplitz(sources)))
    partners = jnp.concatenate([arrived[r, :SRC] for r in range(ROUNDS)], axis=0)
    far = window_sum(correlate(windows, source_toeplitz(partners)))
    rows = jnp.concatenate([own, far], axis=0)
    owners_total = lax.axis_size("chan")
    nbins = owners_total * BINCAP
    bins_parts = [owner[:rows_set] * BINCAP + slot[:rows_set]]
    for r in range(ROUNDS):
        got = arrived[r, SRC].astype(jnp.int32)
        bins_parts.append(got[:rows_set] * BINCAP + got[rows_set : 2 * rows_set])
    bins = jnp.concatenate(bins_parts)
    picks = (bins[None, :] == jnp.arange(nbins, dtype=jnp.int32)[:, None]).astype(jnp.float32)
    local = jnp.dot(picks, rows, precision=lax.Precision.HIGHEST, preferred_element_type=jnp.float32)
    own_bins = owner * BINCAP + slot
    own_counts = jnp.sum(
        (own_bins[None, :] == jnp.arange(nbins, dtype=jnp.int32)[:, None]).astype(jnp.float32), axis=1
    )
    local = local.reshape(owners_total, BINCAP, -1)
    count_cols = jnp.broadcast_to(own_counts.reshape(owners_total, BINCAP, 1), (owners_total, BINCAP, block_width))
    outgoing = jnp.concatenate([local, count_cols], axis=2)
    arrived_sums = lax.all_to_all(outgoing.astype(jnp.bfloat16), "chan", split_axis=0, concat_axis=0, tiled=True)
    arrived_sums = jnp.sum(arrived_sums.astype(jnp.float32), axis=0)
    sums = arrived_sums[:, : local.shape[2]]
    counts = arrived_sums[:, local.shape[2]]
    return sums / jnp.sqrt(jnp.maximum(counts, 1.0))[:, None]


def solution(mesh):
    return jax.shard_map(
        body,
        mesh=mesh,
        in_specs=(P("win", "chan", None), P(), P("chan", None), P("chan")),
        out_specs=P("chan", "win"),
        check_vma=False,
    )
```

```python
import jax
import jax.numpy as jnp
from jax import lax
from jax.sharding import PartitionSpec as P
from jax.experimental import pallas as pl
from jax.experimental.pallas import tpu as pltpu

LAG = 512
SRC = 2
ROUNDS = 2
BINCAP = 4


block_width = 128


def normalize(traces):
    data = traces.astype(jnp.float32)
    scale = lax.rsqrt(jnp.mean(data * data, axis=-1, keepdims=True) + 1e-06)
    return (data * scale).astype(jnp.bfloat16)


def toeplitz_kernel(src_ref, out_ref):
    for q in range(out_ref.shape[1]):
        row = src_ref[0, q : q + 1, :].astype(jnp.float32)
        row = jnp.concatenate([row, jnp.zeros_like(row)], axis=1)
        band = jnp.broadcast_to(row, (block_width, 2 * block_width))
        out_ref[0, q] = pltpu.roll(band, 0, 1, stride=1, stride_axis=0).astype(out_ref.dtype)


def source_toeplitz(sources):
    n, samples = sources.shape
    quota = samples // block_width
    blocks = sources.reshape(n, quota, block_width)
    return pl.pallas_call(
        toeplitz_kernel,
        grid=(n,),
        in_specs=[pl.BlockSpec((1, quota, block_width), lambda s: (s, 0, 0))],
        out_specs=pl.BlockSpec((1, quota, block_width, 2 * block_width), lambda s: (s, 0, 0, 0)),
        out_shape=jax.ShapeDtypeStruct((n, quota, block_width, 2 * block_width), sources.dtype),
    )(blocks)


def receiver_windows(receivers):
    chans, samples = receivers.shape
    quota = samples // block_width
    lag_blocks = 2 * LAG // block_width
    extended = jnp.pad(receivers, ((0, 0), (LAG, LAG + block_width)))
    cells = extended.reshape(chans, -1, block_width)
    doubled = jnp.concatenate([cells[:, :-1], cells[:, 1:]], axis=-1)
    return jnp.stack([doubled[:, p : p + quota] for p in range(lag_blocks)], axis=1)


def correlate(windows, toeplitz):
    return jnp.einsum("cpqw,sqrw->scpr", windows, toeplitz, preferred_element_type=jnp.float32)


def xor_permute(x, mask, axis, shift, width):
    n = lax.axis_size(axis)

    def moved(step):
        return lambda v: lax.ppermute(v, axis, [(i, i ^ step) for i in range(n)])

    branches = [lambda v: v] + [moved(d << shift) for d in range(1, 1 << width)]
    part = jnp.bitwise_and(jnp.right_shift(mask, shift), (1 << width) - 1)
    return lax.switch(part, branches, x)


def exchange(payload, masks, axis):
    n = lax.axis_size(axis)
    bits = n.bit_length() - 1
    full = n - 1
    first_full = masks[0] == full
    other = jnp.bitwise_xor(jnp.bitwise_xor(masks[0], masks[1]), full)
    fixed = jnp.where(first_full, payload[0], payload[1])
    free = jnp.where(first_full, payload[1], payload[0])
    fixed = lax.ppermute(fixed, axis, [(i, i ^ full) for i in range(n)])
    low = min(bits, 4)
    free = xor_permute(free, other, axis, 0, low)
    if bits > low:
        free = xor_permute(free, other, axis, low, bits - low)
    return jnp.stack(
        [jnp.where(first_full, fixed, free), jnp.where(first_full, free, fixed)]
    )


def body(traces, round_masks, row_owner, row_slot):
    wins, chans, samples = traces.shape
    rows_set = SRC * chans
    normed = normalize(traces)[0]
    stride = chans // SRC
    sources = normed[::stride, :]
    owner = row_owner[:, 0]
    slot = row_slot
    label_rows = []
    for r in range(ROUNDS):
        part = slice((r + 1) * rows_set, (r + 2) * rows_set)
        row = jnp.concatenate([owner[part], slot[part]]).astype(jnp.bfloat16)
        row = jnp.pad(row, (0, samples - row.shape[0]))
        label_rows.append(jnp.concatenate([sources, row[None, :]], axis=0))
    payload = jnp.stack(label_rows)
    arrived = exchange(payload, round_masks, "chan")
    windows = receiver_windows(normed)
    scale = 1.0 / jnp.sqrt(jnp.float32(samples))
    wins_total = lax.axis_size("win")

    def window_sum(part):
        part = part.reshape(-1, wins_total, 2 * LAG // wins_total)
        part = lax.all_to_all(part.astype(jnp.bfloat16), "win", split_axis=1, concat_axis=1, tiled=True)
        return jnp.sum(part.astype(jnp.float32), axis=1)

    own = window_sum(correlate(windows, source_toeplitz(sources)))
    partners = jnp.concatenate([arrived[r, :SRC] for r in range(ROUNDS)], axis=0)
    far = window_sum(correlate(windows, source_toeplitz(partners)))
    rows = jnp.concatenate([own, far], axis=0)
    owners_total = lax.axis_size("chan")
    nbins = owners_total * BINCAP
    bins_parts = [owner[:rows_set] * BINCAP + slot[:rows_set]]
    for r in range(ROUNDS):
        got = arrived[r, SRC].astype(jnp.int32)
        bins_parts.append(got[:rows_set] * BINCAP + got[rows_set : 2 * rows_set])
    bins = jnp.concatenate(bins_parts)
    picks = (bins[None, :] == jnp.arange(nbins, dtype=jnp.int32)[:, None]).astype(jnp.float32)
    local = jnp.dot(picks, rows, precision=lax.Precision.HIGH, preferred_element_type=jnp.float32)
    own_bins = owner * BINCAP + slot
    own_counts = jnp.sum(
        (own_bins[None, :] == jnp.arange(nbins, dtype=jnp.int32)[:, None]).astype(jnp.float32), axis=1
    )
    local = local.reshape(owners_total, BINCAP, -1)
    count_cols = jnp.broadcast_to(own_counts.reshape(owners_total, BINCAP, 1), (owners_total, BINCAP, block_width))
    outgoing = jnp.concatenate([local, count_cols], axis=2)
    arrived_sums = lax.all_to_all(outgoing.astype(jnp.bfloat16), "chan", split_axis=0, concat_axis=0, tiled=True)
    arrived_sums = jnp.sum(arrived_sums.astype(jnp.float32), axis=0)
    sums = arrived_sums[:, : local.shape[2]]
    counts = arrived_sums[:, local.shape[2]]
    return sums * (scale / jnp.sqrt(jnp.maximum(counts, 1.0)))[:, None]


def solution(mesh):
    return jax.shard_map(
        body,
        mesh=mesh,
        in_specs=(P("win", "chan", None), P(), P("chan", None), P("chan")),
        out_specs=P("chan", "win"),
        check_vma=False,
    )
```
